512 devices in a mesh: reach: 128 (over z, y, core), ens: 4 (over x).
Axes of the slice: x: 4, y: 4, z: 16, core: 2. Of those that a mesh axis runs over, the one named last changes fastest.
Arguments:
- adjoint: float32 [16, 3, 64, 16384], P('ens', None, None, 'reach'), may hold values from -6 to 6
- momentum: bfloat16 [16, 2, 64, 16384], P('ens', None, None, 'reach'), may hold values from -6 to 6
- friction: float32 [64, 16384], P(None, 'reach'), may hold values from 10 to 100
- roughness: float32 [2048], replicated, may hold values from 0.02 to 0.1
- geometry: float32 [2, 16384], P(None, 'reach'), may hold values from 0.5 to 2
- face_scale: float32 [4, 16384], P(None, 'reach'), may hold values from 0.5 to 2
- vol_blocks: float32 [2, 64, 64], replicated, may hold values from -0.75 to 0.75
- face_blocks: float32 [4, 64, 64], replicated, may hold values from -0.75 to 0.75
- flux_mix: float32 [2, 3, 3], replicated, may hold values from -3.5 to 3.5
- neighbours: int32 [4, 16384], P(None, 'reach'), may hold values from -1 to 16383, as said below
- patch_map: int32 [16384], P('reach'), may hold values from 0 to 2047
- patch_owner: int32 [2048], replicated, may hold values from 0 to 127, as said below
- wet: int32 [16384], P('reach'), may hold values 0 or 1
Outputs:
- finals: float32 [16, 3, 64, 16384], P('ens', None, None, 'reach')
- owned: float32 [4096], P('reach')
The draws below stay inside these ranges and needn't reach their ends.
Inputs may be any that keep to these rules, and one draw needn't show every extreme that they name: `neighbours`: each entry is -1 or an element index at most 32 positions from the element's own index. `patch_owner`: each owner holds at most 32 patches, and some owner holds exactly 32.
All inputs are finite; a program needn't handle non-finite values. No bound on the sum of `wet` on one device may be relied on, other than what follows from the above.
Results may differ from the reference program's by a relative error of at most 0.0003.
Values sent between devices are 32-bit elements; how exact they have to be, the bound alone decides.
No kernel may reach another device: no remote copies, remote signals or barrier semaphores. Data moves between devices by JAX's collectives and lax.ppermute only.
A program may use at most 64 MiB of HBM per device.

```python
import math
import jax
import jax.numpy as jnp
from jax import lax

P_SIZE = 64
RIVW = 32
E_DEV = 128
PATCH_DEV = 16
STEPS = 2
OWN_MAX = 32
NE = 16384
MEMBERS = 16
NPATCH = 2048
N_REACH = 128


def draw_neighbours(key, part):
    subkeys = jax.random.split(key, 2)
    cells = jnp.arange(NE, dtype=jnp.int32)
    jitter = jax.random.randint(subkeys[0], (2, NE), 0, RIVW // 4 + 1)
    forced = cells % 64 == 5
    jitter = jnp.where(forced[None, :], 0, jitter)
    forward_link = cells + RIVW - jitter[0]
    backward_link = cells - RIVW + jitter[1]
    upper_link = jnp.where(cells % RIVW == RIVW - 1, -1, cells + 1)
    lower_link = jnp.where(cells % RIVW == 0, -1, cells - 1)
    link_table = jnp.stack([forward_link, backward_link, upper_link, lower_link])
    wall_mask = jax.random.randint(subkeys[1], (4, NE), 0, 10) == 0
    wall_mask = wall_mask & jnp.logical_not(forced)[None, :]
    link_table = jnp.where(wall_mask, -1, link_table)
    link_table = jnp.where((link_table < 0) | (link_table >= NE), -1, link_table)
    return link_table.astype(jnp.int32)


def draw_patch_map(key, part):
    patch_len = E_DEV // PATCH_DEV
    cells = jnp.arange(NE, dtype=jnp.int32)
    shift_val = jax.random.randint(key, (NE,), -(patch_len // 4), patch_len // 4 + 1)
    return jnp.clip((cells + shift_val) // patch_len, 0, NPATCH - 1).astype(jnp.int32)


def draw_patch_owner(key, part):
    subkeys = jax.random.split(key, 3)
    owner_count = NE // E_DEV
    slot_count = owner_count * OWN_MAX
    chosen_owner = jax.random.randint(subkeys[0], (), 0, owner_count)
    slot_ids = jnp.arange(slot_count, dtype=jnp.int32)
    ranking = jax.random.permutation(subkeys[1], slot_count).astype(jnp.int32)
    scores = jnp.where(slot_ids // OWN_MAX == chosen_owner, slot_ids - slot_count, ranking)
    ordering = jnp.argsort(scores, stable=True)
    picked = (ordering[:NPATCH] // OWN_MAX).astype(jnp.int32)
    return jax.random.permutation(subkeys[2], picked).astype(jnp.int32)


def place_ends(drawn, stream_key, low, top_value):
    spot = [jax.random.randint(jax.random.fold_in(stream_key, axis), (), 0, length) for axis, length in enumerate(drawn.shape)]
    main_axis = drawn.shape.index(max(drawn.shape))
    beside = spot[:main_axis] + [(spot[main_axis] + 1) % drawn.shape[main_axis]] + spot[main_axis + 1:]
    return drawn.at[tuple(spot)].set(low).at[tuple(beside)].set(top_value)


def levels(key, shape, cuts, low, high):
    factor_of = 1.0
    for dim, shards_of in cuts:
        steps = jax.random.uniform(jax.random.fold_in(jax.random.fold_in(key, 6), dim), (shards_of,), jnp.float32, low / len(cuts), high / len(cuts))
        factor_of = factor_of * jnp.repeat(jnp.exp(steps), shape[dim] // shards_of).reshape((-1,) + (1,) * (len(shape) - 1 - dim))
    return factor_of


def gaussian(key, dims, spread, bound, pieces=(), kind=jnp.bfloat16):
    result = jax.random.normal(key, dims, jnp.float32) * spread
    if len(pieces) > 0:
        result = levels(key, dims, pieces, -0.22, 0.18) * result
    return jnp.clip(result, min=-bound, max=bound).astype(kind)


def setup_inputs(seed: int = 0) -> dict:
    splits = jax.random.split(jax.random.key(seed), 14)
    return {
        "adjoint": gaussian(splits[0], (MEMBERS, 3, P_SIZE, NE), 1.0, 6.0, ((0, 4), (3, 128)), jnp.float32),
        "momentum": gaussian(splits[1], (MEMBERS, 2, P_SIZE, NE), 1.0, 6.0, ((0, 4), (3, 128))),
        "friction": jnp.clip(jnp.exp(math.log(100.0) - 2.3025851 * jax.random.uniform(splits[2], (P_SIZE, NE), jnp.float32) ** levels(splits[2], (P_SIZE, NE), ((1, 128),), -0.2, 0.2)), 10.0, 100.0),
        "roughness": jnp.clip(jnp.exp(jax.random.uniform(splits[3], (NPATCH,), jnp.float32, math.log(0.02), math.log(0.1))), 0.02, 0.1),
        "geometry": jnp.clip(0.5 + 1.5 * jax.random.uniform(splits[4], (2, NE), jnp.float32) ** levels(splits[4], (2, NE), ((1, 128),), -0.2, 0.2), 0.5, 2.0),
        "face_scale": jnp.clip(jnp.exp(math.log(2.0) - 1.3862944 * jax.random.uniform(splits[5], (4, NE), jnp.float32) ** levels(splits[5], (4, NE), ((1, 128),), -0.2, 0.2)), 0.5, 2.0),
        "vol_blocks": gaussian(splits[6], (2, P_SIZE, P_SIZE), P_SIZE ** -0.5, 0.75, (), jnp.float32),
        "face_blocks": gaussian(splits[7], (4, P_SIZE, P_SIZE), P_SIZE ** -0.5, 0.75, (), jnp.float32),
        "flux_mix": gaussian(splits[8], (2, 3, 3), 3 ** -0.5, 3.5, (), jnp.float32),
        "neighbours": draw_neighbours(jax.random.fold_in(splits[13], 71), 0),
        "patch_map": draw_patch_map(jax.random.fold_in(splits[13], 71), 0),
        "patch_owner": draw_patch_owner(jax.random.fold_in(splits[13], 71), 0),
        "wet": place_ends((jax.random.randint(splits[12], (NE,), 0, 4) < 3).astype(jnp.int32), jax.random.fold_in(splits[12], 1), 0, 1),
    }


TIME_STEP = 0.05
FINEST = lax.Precision.HIGHEST


def apply_block(block, values):
    return jnp.einsum('qp,mcpe->mcqe', block, values, precision=FINEST)


def mix_flux(matrix, values):
    return jnp.einsum('dc,mdpe->mcpe', matrix, values, precision=FINEST)


def adjoint_rhs(lam_ext, anchor, offset, extent, links, geo_sel, face_sel, coef_sel, wet_sel, vol_blocks, face_blocks, flux_mix):
    inside = lax.slice_in_dim(lam_ext, offset, offset + extent, axis=3)
    summed = geo_sel[0] * apply_block(vol_blocks[0], mix_flux(flux_mix[0], inside))
    summed = summed + geo_sel[1] * apply_block(vol_blocks[1], mix_flux(flux_mix[1], inside))
    span_len = lam_ext.shape[3]
    for face_id in range(4):
        target = links[face_id]
        position = jnp.clip(target - anchor, 0, span_len - 1).astype(jnp.int32)
        remote = jnp.take(lam_ext, position, axis=3)
        jump_val = jnp.where(target >= 0, remote - inside, jnp.zeros_like(inside))
        summed = summed + face_sel[face_id] * apply_block(face_blocks[face_id], jump_val)
    damping = -coef_sel * inside[:, 1:3]
    summed = summed + jnp.concatenate([jnp.zeros_like(inside[:, :1]), damping], axis=1)
    return wet_sel * summed


def friction_work(adjoint_now, moment, weights):
    return jnp.sum(weights * (moment[:, 0] * adjoint_now[:, 1] + moment[:, 1] * adjoint_now[:, 2]), axis=1)


def owner_slots(patch_owner, owner_count, capacity):
    table = (patch_owner[:, None] == jnp.arange(owner_count, dtype=jnp.int32)[None, :]).astype(jnp.int32)
    ranks = jnp.cumsum(table, axis=0) - 1
    ranking = jnp.sum(ranks * table, axis=1)
    return (patch_owner * capacity + ranking).astype(jnp.int32)


def reference(adjoint, momentum, friction, roughness, geometry, face_scale, vol_blocks, face_blocks, flux_mix, neighbours, patch_map, patch_owner, wet):
    patch_rough = roughness[patch_map]
    coef_all = patch_rough[None, :] ** 2 * friction
    wet_all = wet.astype(jnp.float32)
    weights = wet_all * (-2.0 * patch_rough) * friction

    def member(member_pair):
        adjoint_now = member_pair[0][None]
        moment = member_pair[1][None].astype(jnp.float32)
        accrued = jnp.zeros((1, NE), jnp.float32)
        for step_no in range(STEPS):
            accrued = accrued + friction_work(adjoint_now, moment, weights)
            slope = adjoint_rhs(adjoint_now, 0, 0, NE, neighbours, geometry, face_scale, coef_all, wet_all, vol_blocks, face_blocks, flux_mix)
            halfway = adjoint_now + TIME_STEP * slope
            accrued = accrued + friction_work(halfway, moment, weights)
            slope = adjoint_rhs(halfway, 0, 0, NE, neighbours, geometry, face_scale, coef_all, wet_all, vol_blocks, face_blocks, flux_mix)
            adjoint_now = 0.5 * adjoint_now + 0.5 * (halfway + TIME_STEP * slope)
        return adjoint_now[0], accrued[0]

    finals, accrued = lax.map(member, (adjoint, momentum))
    per_element = jnp.sum(accrued, axis=0)
    patch_sums = jax.ops.segment_sum(per_element, patch_map, num_segments=NPATCH) / (MEMBERS * P_SIZE)
    slots = owner_slots(patch_owner, N_REACH, OWN_MAX)
    owned = jnp.zeros((N_REACH * OWN_MAX,), jnp.float32).at[slots].set(patch_sums)
    return (finals, owned)
```

```python
import jax
import jax.numpy as jnp
from jax import lax
from jax.sharding import PartitionSpec as P

RIVW = 32
STEPS = 2
OWN_MAX = 32


TIME_STEP = 0.05
FINEST = lax.Precision.HIGHEST


def extended(cells, sides, width):
    for axis, dim in sides:
        count = lax.axis_size(axis)
        ends = count - 1
        head = lax.slice_in_dim(cells, 0, width, axis=dim)
        tail = lax.slice_in_dim(cells, cells.shape[dim] - width, cells.shape[dim], axis=dim)
        cells = jnp.concatenate(
            [
                lax.ppermute(tail, axis, [(i, (i + 1) % count) for i in range(ends)]),
                cells,
                lax.ppermute(head, axis, [((i + 1) % count, i) for i in range(ends)]),
            ],
            axis=dim,
        )
    return cells


def apply_block(block, values):
    return jnp.einsum("qp,mcpe->mcqe", block, values, precision=FINEST)


def mix_flux(matrix, values):
    return jnp.einsum("dc,mdpe->mcpe", matrix, values, precision=FINEST)


def adjoint_rhs(
    lam_ext,
    anchor,
    offset,
    extent,
    links,
    geo_sel,
    face_sel,
    coef_sel,
    wet_sel,
    vol_blocks,
    face_blocks,
    flux_mix,
):
    inside = lax.slice_in_dim(lam_ext, offset, offset + extent, axis=3)
    summed = geo_sel[0] * apply_block(vol_blocks[0], mix_flux(flux_mix[0], inside))
    summed = summed + geo_sel[1] * apply_block(vol_blocks[1], mix_flux(flux_mix[1], inside))
    span_len = lam_ext.shape[3]
    for face_id in range(4):
        target = links[face_id]
        position = jnp.clip(target - anchor, 0, span_len - 1)
        remote = jnp.take(lam_ext, position, axis=3)
        jump_val = jnp.where(target >= 0, remote - inside, jnp.zeros_like(inside))
        summed = summed + face_sel[face_id] * apply_block(face_blocks[face_id], jump_val)
    damping = -coef_sel * inside[:, 1:3]
    summed = summed + jnp.concatenate([jnp.zeros_like(inside[:, :1]), damping], axis=1)
    return wet_sel * summed


def friction_work(adjoint_now, moment, weights):
    return jnp.sum(
        weights * (moment[:, 0] * adjoint_now[:, 1] + moment[:, 1] * adjoint_now[:, 2]), axis=1
    )


def owner_slots(patch_owner, owner_count, capacity):
    table = (patch_owner[:, None] == jnp.arange(owner_count, dtype=jnp.int32)[None, :]).astype(
        jnp.int32
    )
    ranks = jnp.cumsum(table, axis=0) - 1
    ranking = jnp.sum(ranks * table, axis=1)
    return patch_owner * capacity + ranking


def shards(
    adjoint,
    momentum,
    friction,
    roughness,
    geometry,
    face_scale,
    vol_blocks,
    face_blocks,
    flux_mix,
    neighbours,
    patch_map,
    patch_owner,
    wet,
):
    elements = adjoint.shape[3]
    global_start = lax.axis_index("reach") * elements
    patch_rough = roughness[patch_map]
    coef_own = patch_rough[None, :] ** 2 * friction
    wet_own = wet.astype(jnp.float32)
    weights = wet_own * (-2.0 * patch_rough) * friction
    moment = momentum.astype(jnp.float32)
    adjoint_now = adjoint
    accrued = jnp.zeros((adjoint.shape[0], elements), jnp.float32)

    def section_slope(state):
        rim_ext = extended(state, (("reach", 3),), RIVW)
        return adjoint_rhs(
            rim_ext,
            global_start - RIVW,
            RIVW,
            elements,
            neighbours,
            geometry,
            face_scale,
            coef_own,
            wet_own,
            vol_blocks,
            face_blocks,
            flux_mix,
        )

    for step_no in range(STEPS):
        accrued = accrued + friction_work(adjoint_now, moment, weights)
        halfway = adjoint_now + TIME_STEP * section_slope(adjoint_now)
        accrued = accrued + friction_work(halfway, moment, weights)
        adjoint_now = 0.5 * adjoint_now + 0.5 * (halfway + TIME_STEP * section_slope(halfway))
    per_element = jnp.sum(accrued, axis=0)
    patch_count = roughness.shape[0]
    members = adjoint.shape[0] * lax.axis_size("ens")
    patch_ids = jnp.arange(patch_count, dtype=jnp.int32)
    hit = patch_map[None, :] == patch_ids[:, None]
    partial = jnp.sum(jnp.where(hit, per_element[None, :], 0.0), axis=1)
    patch_sums = lax.psum(partial, ("reach", "ens")) / (members * adjoint.shape[2])
    me = lax.axis_index("reach")
    mine = patch_owner == me
    rank = jnp.cumsum(mine.astype(jnp.int32)) - 1
    slot_ids = jnp.arange(OWN_MAX, dtype=jnp.int32)
    pick = mine[None, :] & (rank[None, :] == slot_ids[:, None])
    owned = jnp.sum(jnp.where(pick, patch_sums[None, :], 0.0), axis=1)
    return (adjoint_now, owned)


def solution(mesh):
    return jax.shard_map(
        shards,
        mesh=mesh,
        in_specs=(
            P("ens", None, None, "reach"),
            P("ens", None, None, "reach"),
            P(None, "reach"),
            P(),
            P(None, "reach"),
            P(None, "reach"),
            P(),
            P(),
            P(),
            P(None, "reach"),
            P("reach"),
            P(),
            P("reach"),
        ),
        out_specs=(P("ens", None, None, "reach"), P("reach")),
        check_vma=False,
    )
```

```python
import jax
import jax.numpy as jnp
from jax import lax
from jax.sharding import PartitionSpec as P

RIVW = 32
STEPS = 2
OWN_MAX = 32


TIME_STEP = 0.05
FINEST = lax.Precision.HIGHEST


def extended(cells, sides, width):
    for axis, dim in sides:
        count = lax.axis_size(axis)
        ends = count - 1
        head = lax.slice_in_dim(cells, 0, width, axis=dim)
        tail = lax.slice_in_dim(cells, cells.shape[dim] - width, cells.shape[dim], axis=dim)
        cells = jnp.concatenate(
            [
                lax.ppermute(tail, axis, [(i, (i + 1) % count) for i in range(ends)]),
                cells,
                lax.ppermute(head, axis, [((i + 1) % count, i) for i in range(ends)]),
            ],
            axis=dim,
        )
    return cells


def apply_block(block, values):
    return jnp.einsum("qp,mcpe->mcqe", block, values, precision=FINEST)


def mix_flux(matrix, values):
    return jnp.einsum("dc,mdpe->mcpe", matrix, values, precision=FINEST)


def adjoint_rhs(
    lam_ext,
    anchor,
    offset,
    extent,
    links,
    geo_sel,
    face_sel,
    coef_sel,
    wet_sel,
    vol_blocks,
    face_blocks,
    flux_mix,
):
    inside = lax.slice_in_dim(lam_ext, offset, offset + extent, axis=3)
    summed = geo_sel[0] * apply_block(vol_blocks[0], mix_flux(flux_mix[0], inside))
    summed = summed + geo_sel[1] * apply_block(vol_blocks[1], mix_flux(flux_mix[1], inside))
    span_len = lam_ext.shape[3]
    for face_id in range(4):
        target = links[face_id]
        position = jnp.clip(target - anchor, 0, span_len - 1)
        remote = jnp.take(lam_ext, position, axis=3)
        jump_val = jnp.where(target >= 0, remote - inside, jnp.zeros_like(inside))
        summed = summed + face_sel[face_id] * apply_block(face_blocks[face_id], jump_val)
    damping = -coef_sel * inside[:, 1:3]
    summed = summed + jnp.concatenate([jnp.zeros_like(inside[:, :1]), damping], axis=1)
    return wet_sel * summed


def friction_work(adjoint_now, moment, weights):
    return jnp.sum(
        weights * (moment[:, 0] * adjoint_now[:, 1] + moment[:, 1] * adjoint_now[:, 2]), axis=1
    )


def owner_slots(patch_owner, owner_count, capacity):
    table = (patch_owner[:, None] == jnp.arange(owner_count, dtype=jnp.int32)[None, :]).astype(
        jnp.int32
    )
    ranks = jnp.cumsum(table, axis=0) - 1
    ranking = jnp.sum(ranks * table, axis=1)
    return patch_owner * capacity + ranking


def shards(
    adjoint,
    momentum,
    friction,
    roughness,
    geometry,
    face_scale,
    vol_blocks,
    face_blocks,
    flux_mix,
    neighbours,
    patch_map,
    patch_owner,
    wet,
):
    elements = adjoint.shape[3]
    global_start = lax.axis_index("reach") * elements
    patch_rough = roughness[patch_map]
    coef_own = patch_rough[None, :] ** 2 * friction
    wet_own = wet.astype(jnp.float32)
    weights = wet_own * (-2.0 * patch_rough) * friction
    moment = momentum.astype(jnp.float32)
    adjoint_now = adjoint
    accrued = jnp.zeros((adjoint.shape[0], elements), jnp.float32)

    def section_slope(state):
        rim_ext = extended(state, (("reach", 3),), RIVW)
        return adjoint_rhs(
            rim_ext,
            global_start - RIVW,
            RIVW,
            elements,
            neighbours,
            geometry,
            face_scale,
            coef_own,
            wet_own,
            vol_blocks,
            face_blocks,
            flux_mix,
        )

    for step_no in range(STEPS):
        accrued = accrued + friction_work(adjoint_now, moment, weights)
        halfway = adjoint_now + TIME_STEP * section_slope(adjoint_now)
        accrued = accrued + friction_work(halfway, moment, weights)
        adjoint_now = 0.5 * adjoint_now + 0.5 * (halfway + TIME_STEP * section_slope(halfway))
    per_element = jnp.sum(accrued, axis=0)
    owner_count = lax.axis_size("reach")
    members = adjoint.shape[0] * lax.axis_size("ens")
    patch_count = roughness.shape[0]
    patch_ids = jnp.arange(patch_count, dtype=jnp.int32)
    owner_e = patch_owner[patch_map]
    earlier = (patch_ids[None, :] < patch_map[:, None]) & (patch_owner[None, :] == owner_e[:, None])
    rank_e = jnp.sum(earlier.astype(jnp.int32), axis=1)
    slot_e = owner_e * OWN_MAX + rank_e
    slot_ids = jnp.arange(owner_count * OWN_MAX, dtype=jnp.int32)
    hit = slot_e[None, :] == slot_ids[:, None]
    send = jnp.sum(jnp.where(hit, per_element[None, :], 0.0), axis=1).reshape(owner_count, OWN_MAX)
    got = lax.all_to_all(send, "reach", 0, 0, tiled=True)
    owned = lax.psum(jnp.sum(got, axis=0), "ens") / (members * adjoint.shape[2])
    return (adjoint_now, owned)


def solution(mesh):
    return jax.shard_map(
        shards,
        mesh=mesh,
        in_specs=(
            P("ens", None, None, "reach"),
            P("ens", None, None, "reach"),
            P(None, "reach"),
            P(),
            P(None, "reach"),
            P(None, "reach"),
            P(),
            P(),
            P(),
            P(None, "reach"),
            P("reach"),
            P(),
            P("reach"),
        ),
        out_specs=(P("ens", None, None, "reach"), P("reach")),
        check_vma=False,
    )
```

```python
import functools

import jax
import jax.numpy as jnp
from jax import lax
from jax.experimental import pallas as pl
from jax.experimental.pallas import tpu as pltpu
from jax.sharding import PartitionSpec as P

RIVW = 32
STEPS = 2
OWN_MAX = 32
PAD = 128

TIME_STEP = 0.05


def halos(cells, axis, width):
    count = lax.axis_size(axis)
    ends = count - 1
    head = lax.slice_in_dim(cells, 0, width, axis=1)
    tail = lax.slice_in_dim(cells, cells.shape[1] - width, cells.shape[1], axis=1)
    left = lax.ppermute(tail, axis, [(i, (i + 1) % count) for i in range(ends)])
    right = lax.ppermute(head, axis, [((i + 1) % count, i) for i in range(ends)])
    return left, right


def rhs_kernel(members, nodes, elems, fm_ref, ext_ref, sel_ref, msk_ref, fs_ref, geo_ref, coef_ref,
               wet_ref, w_ref, out_ref, x_ref):
    dot = functools.partial(jnp.dot, preferred_element_type=jnp.float32, precision=lax.Precision.HIGHEST)
    ext = ext_ref[...]
    own = ext[:, PAD:PAD + elems]
    sel = sel_ref[...]
    gathered = dot(ext, sel)
    blocks = members * 3
    for f in range(4):
        jump = (gathered[:, f * elems:(f + 1) * elems] - msk_ref[f:f + 1, :] * own) * fs_ref[f:f + 1, :]
        for b in range(blocks):
            x_ref[(2 + f) * nodes:(3 + f) * nodes, b * elems:(b + 1) * elems] = jump[b * nodes:(b + 1) * nodes]
    for m in range(members):
        comps = [own[(m * 3 + d) * nodes:(m * 3 + d + 1) * nodes] for d in range(3)]
        for dirn in range(2):
            for c in range(3):
                v = (fm_ref[dirn * 9 + c] * comps[0] + fm_ref[dirn * 9 + 3 + c] * comps[1]
                     + fm_ref[dirn * 9 + 6 + c] * comps[2])
                b = m * 3 + c
                x_ref[dirn * nodes:(dirn + 1) * nodes, b * elems:(b + 1) * elems] = geo_ref[dirn:dirn + 1, :] * v
    out = dot(w_ref[...], x_ref[...])
    wet = wet_ref[...]
    coef = coef_ref[...]
    for b in range(blocks):
        r = out[:, b * elems:(b + 1) * elems]
        if b % 3 > 0:
            r = r - coef * own[b * nodes:(b + 1) * nodes]
        out_ref[b * nodes:(b + 1) * nodes, :] = wet * r


def rhs_call(fm, ext, sel, msk, fs, geo, coef, wet, w, members, nodes, elems):
    rows = members * 3 * nodes
    vmem = pl.BlockSpec(memory_space=pltpu.VMEM)
    return pl.pallas_call(
        functools.partial(rhs_kernel, members, nodes, elems),
        out_shape=jax.ShapeDtypeStruct((rows, elems), jnp.float32),
        in_specs=[pl.BlockSpec(memory_space=pltpu.SMEM)] + [vmem] * 8,
        out_specs=vmem,
        scratch_shapes=[pltpu.VMEM((6 * nodes, members * 3 * elems), jnp.float32)],
    )(fm, ext, sel, msk, fs, geo, coef, wet, w)


def friction_work(adjoint_now, moment, weights):
    return jnp.sum(
        weights * (moment[:, 0] * adjoint_now[:, 1] + moment[:, 1] * adjoint_now[:, 2]), axis=1
    )


def shards(
    adjoint,
    momentum,
    friction,
    roughness,
    geometry,
    face_scale,
    vol_blocks,
    face_blocks,
    flux_mix,
    neighbours,
    patch_map,
    patch_owner,
    wet,
):
    members, comps, nodes, elems = adjoint.shape
    rows = members * comps * nodes
    global_start = lax.axis_index("reach") * elems
    patch_rough = roughness[patch_map]
    coef_own = patch_rough[None, :] ** 2 * friction
    wet_own = wet.astype(jnp.float32)
    weights = wet_own * (-2.0 * patch_rough) * friction
    moment = momentum.astype(jnp.float32)

    width = elems + 2 * PAD
    position = neighbours - global_start + PAD
    valid = neighbours >= 0
    src = jnp.arange(width, dtype=jnp.int32)
    sel = (src[:, None, None] == position[None, :, :]) & valid[None, :, :]
    sel = sel.reshape(width, 4 * elems).astype(jnp.float32)
    msk = valid.astype(jnp.float32)
    blocks = jnp.concatenate([vol_blocks[0], vol_blocks[1]] + [face_blocks[f] for f in range(4)], axis=1)
    fm = flux_mix.reshape(-1)
    wet_row = wet_own[None, :]

    def section_slope(state):
        flat = state.reshape(rows, elems)
        left, right = halos(flat, "reach", RIVW)
        zeros = jnp.zeros((rows, PAD - RIVW), jnp.float32)
        ext = jnp.concatenate([zeros, left, flat, right, zeros], axis=1)
        slope = rhs_call(fm, ext, sel, msk, face_scale, geometry, coef_own, wet_row, blocks,
                         members, nodes, elems)
        return slope.reshape(members, comps, nodes, elems)

    adjoint_now = adjoint
    accrued = jnp.zeros((members, elems), jnp.float32)
    for step_no in range(STEPS):
        accrued = accrued + friction_work(adjoint_now, moment, weights)
        halfway = adjoint_now + TIME_STEP * section_slope(adjoint_now)
        accrued = accrued + friction_work(halfway, moment, weights)
        adjoint_now = 0.5 * adjoint_now + 0.5 * (halfway + TIME_STEP * section_slope(halfway))
    per_element = jnp.sum(accrued, axis=0)
    owner_count = lax.axis_size("reach")
    total_members = members * lax.axis_size("ens")
    patch_count = roughness.shape[0]
    patch_ids = jnp.arange(patch_count, dtype=jnp.int32)
    owner_e = patch_owner[patch_map]
    earlier = (patch_ids[None, :] < patch_map[:, None]) & (patch_owner[None, :] == owner_e[:, None])
    rank_e = jnp.sum(earlier.astype(jnp.int32), axis=1)
    slot_e = owner_e * OWN_MAX + rank_e
    slot_ids = jnp.arange(owner_count * OWN_MAX, dtype=jnp.int32)
    hit = slot_e[None, :] == slot_ids[:, None]
    send = jnp.sum(jnp.where(hit, per_element[None, :], 0.0), axis=1).reshape(owner_count, OWN_MAX)
    got = lax.all_to_all(send, "reach", 0, 0, tiled=True)
    owned = lax.psum(jnp.sum(got, axis=0), "ens") / (total_members * nodes)
    return (adjoint_now, owned)


def solution(mesh):
    return jax.shard_map(
        shards,
        mesh=mesh,
        in_specs=(
            P("ens", None, None, "reach"),
            P("ens", None, None, "reach"),
            P(None, "reach"),
            P(),
            P(None, "reach"),
            P(None, "reach"),
            P(),
            P(),
            P(),
            P(None, "reach"),
            P("reach"),
            P(),
            P("reach"),
        ),
        out_specs=(P("ens", None, None, "reach"), P("reach")),
        check_vma=False,
    )
```

```python
import functools

import jax
import jax.numpy as jnp
from jax import lax
from jax.experimental import pallas as pl
from jax.experimental.pallas import tpu as pltpu
from jax.sharding import PartitionSpec as P

RIVW = 32
STEPS = 2
OWN_MAX = 32

TIME_STEP = 0.05


def halos(cells, axis, width):
    count = lax.axis_size(axis)
    ends = count - 1
    head = lax.slice_in_dim(cells, 0, width, axis=1)
    tail = lax.slice_in_dim(cells, cells.shape[1] - width, cells.shape[1], axis=1)
    left = lax.ppermute(tail, axis, [(i, (i + 1) % count) for i in range(ends)])
    right = lax.ppermute(head, axis, [((i + 1) % count, i) for i in range(ends)])
    return left, right


def rhs_kernel(members, nodes, elems, mode, fm_ref, own_ref, left_ref, right_ref, base_ref, sel_ref, sell_ref,
               selr_ref, msk_ref, fs_ref, geo_ref, coef_ref, wet_ref, w_ref, out_ref, x_ref):
    dot = functools.partial(jnp.dot, preferred_element_type=jnp.float32, precision=lax.Precision.HIGHEST)
    own = own_ref[...]
    gathered = dot(own, sel_ref[...]) + dot(left_ref[...], sell_ref[...]) + dot(right_ref[...], selr_ref[...])
    blocks = members * 3
    for f in range(4):
        jump = (gathered[:, f * elems:(f + 1) * elems] - msk_ref[f:f + 1, :] * own) * fs_ref[f:f + 1, :]
        for b in range(blocks):
            x_ref[(2 + f) * nodes:(3 + f) * nodes, b * elems:(b + 1) * elems] = jump[b * nodes:(b + 1) * nodes]
    for m in range(members):
        comps = [own[(m * 3 + d) * nodes:(m * 3 + d + 1) * nodes] for d in range(3)]
        for dirn in range(2):
            for c in range(3):
                v = (fm_ref[dirn * 9 + c] * comps[0] + fm_ref[dirn * 9 + 3 + c] * comps[1]
                     + fm_ref[dirn * 9 + 6 + c] * comps[2])
                b = m * 3 + c
                x_ref[dirn * nodes:(dirn + 1) * nodes, b * elems:(b + 1) * elems] = geo_ref[dirn:dirn + 1, :] * v
    out = dot(w_ref[...], x_ref[...])
    wet = wet_ref[...]
    coef = coef_ref[...]
    for b in range(blocks):
        rows = slice(b * nodes, (b + 1) * nodes)
        r = out[:, b * elems:(b + 1) * elems]
        if b % 3 > 0:
            r = r - coef * own[rows]
        stepped = own[rows] + TIME_STEP * (wet * r)
        if mode == 1:
            stepped = 0.5 * base_ref[rows, :] + 0.5 * stepped
        out_ref[rows, :] = stepped


def rhs_call(mode, fm, own, left, right, base, sel, sell, selr, msk, fs, geo, coef, wet, w, members, nodes, elems):
    rows = members * 3 * nodes
    vmem = pl.BlockSpec(memory_space=pltpu.VMEM)
    return pl.pallas_call(
        functools.partial(rhs_kernel, members, nodes, elems, mode),
        out_shape=jax.ShapeDtypeStruct((rows, elems), jnp.float32),
        in_specs=[pl.BlockSpec(memory_space=pltpu.SMEM)] + [vmem] * 13,
        out_specs=vmem,
        scratch_shapes=[pltpu.VMEM((6 * nodes, members * 3 * elems), jnp.float32)],
    )(fm, own, left, right, base, sel, sell, selr, msk, fs, geo, coef, wet, w)


def friction_work(adjoint_now, moment, weights):
    return jnp.sum(
        weights * (moment[:, 0] * adjoint_now[:, 1] + moment[:, 1] * adjoint_now[:, 2]), axis=1
    )


def shards(
    adjoint,
    momentum,
    friction,
    roughness,
    geometry,
    face_scale,
    vol_blocks,
    face_blocks,
    flux_mix,
    neighbours,
    patch_map,
    patch_owner,
    wet,
):
    members, comps, nodes, elems = adjoint.shape
    rows = members * comps * nodes
    global_start = lax.axis_index("reach") * elems
    patch_rough = roughness[patch_map]
    coef_own = patch_rough[None, :] ** 2 * friction
    wet_own = wet.astype(jnp.float32)
    weights = wet_own * (-2.0 * patch_rough) * friction
    moment = momentum.astype(jnp.float32)

    width = elems + 2 * RIVW
    position = neighbours - global_start + RIVW
    valid = neighbours >= 0
    src = jnp.arange(width, dtype=jnp.int32)
    sel = (src[:, None, None] == position[None, :, :]) & valid[None, :, :]
    sel = sel.reshape(width, 4 * elems).astype(jnp.float32)
    sel_left = sel[:RIVW]
    sel_own = sel[RIVW:RIVW + elems]
    sel_right = sel[RIVW + elems:]
    msk = valid.astype(jnp.float32)
    blocks = jnp.concatenate([vol_blocks[0], vol_blocks[1]] + [face_blocks[f] for f in range(4)], axis=1)
    fm = flux_mix.reshape(-1)
    wet_row = wet_own[None, :]

    def stage(mode, state, base):
        flat = state.reshape(rows, elems)
        left, right = halos(flat, "reach", RIVW)
        stepped = rhs_call(mode, fm, flat, left, right, base.reshape(rows, elems), sel_own, sel_left, sel_right,
                           msk, face_scale, geometry, coef_own, wet_row, blocks, members, nodes, elems)
        return stepped.reshape(members, comps, nodes, elems)

    adjoint_now = adjoint
    accrued = jnp.zeros((members, elems), jnp.float32)
    for step_no in range(STEPS):
        accrued = accrued + friction_work(adjoint_now, moment, weights)
        halfway = stage(0, adjoint_now, adjoint_now)
        accrued = accrued + friction_work(halfway, moment, weights)
        adjoint_now = stage(1, halfway, adjoint_now)
    per_element = jnp.sum(accrued, axis=0)
    owner_count = lax.axis_size("reach")
    total_members = members * lax.axis_size("ens")
    patch_count = roughness.shape[0]
    patch_ids = jnp.arange(patch_count, dtype=jnp.int32)
    owner_e = patch_owner[patch_map]
    earlier = (patch_ids[None, :] < patch_map[:, None]) & (patch_owner[None, :] == owner_e[:, None])
    rank_e = jnp.sum(earlier.astype(jnp.int32), axis=1)
    slot_e = owner_e * OWN_MAX + rank_e
    slot_ids = jnp.arange(owner_count * OWN_MAX, dtype=jnp.int32)
    hit = slot_e[None, :] == slot_ids[:, None]
    send = jnp.sum(jnp.where(hit, per_element[None, :], 0.0), axis=1).reshape(owner_count, OWN_MAX)
    got = lax.all_to_all(send, "reach", 0, 0, tiled=True)
    owned = lax.psum(jnp.sum(got, axis=0), "ens") / (total_members * nodes)
    return (adjoint_now, owned)


def solution(mesh):
    return jax.shard_map(
        shards,
        mesh=mesh,
        in_specs=(
            P("ens", None, None, "reach"),
            P("ens", None, None, "reach"),
            P(None, "reach"),
            P(),
            P(None, "reach"),
            P(None, "reach"),
            P(),
            P(),
            P(),
            P(None, "reach"),
            P("reach"),
            P(),
            P("reach"),
        ),
        out_specs=(P("ens", None, None, "reach"), P("reach")),
        check_vma=False,
    )
```

```python
import functools

import jax
import jax.numpy as jnp
from jax import lax
from jax.experimental import pallas as pl
from jax.experimental.pallas import tpu as pltpu
from jax.sharding import PartitionSpec as P

RIVW = 32
STEPS = 2
OWN_MAX = 32

TIME_STEP = 0.05


def halos(cells, axis, width):
    count = lax.axis_size(axis)
    ends = count - 1
    head = lax.slice_in_dim(cells, 0, width, axis=1)
    tail = lax.slice_in_dim(cells, cells.shape[1] - width, cells.shape[1], axis=1)
    left = lax.ppermute(tail, axis, [(i, (i + 1) % count) for i in range(ends)])
    right = lax.ppermute(head, axis, [((i + 1) % count, i) for i in range(ends)])
    return left, right


def rhs_kernel(members, nodes, elems, mode, work_in, work_out, fm_ref, own_ref, left_ref, right_ref, base_ref,
               sel_ref, msk_ref, fs_ref, geo_ref, coef_ref, wet_ref, w_ref, mom_ref, wts_ref, acc_ref,
               out_ref, acc_out_ref, ext_ref, x_ref):
    dot = functools.partial(jnp.dot, preferred_element_type=jnp.float32, precision=lax.Precision.HIGHEST)
    rows = own_ref.shape[0]
    halo = left_ref.shape[1]
    own = own_ref[...]
    ext_ref[:, 0:elems] = own
    ext_ref[:, elems:3 * elems] = jnp.zeros((rows, 2 * elems), jnp.float32)
    ext_ref[:, elems:elems + halo] = left_ref[...]
    ext_ref[:, 2 * elems:2 * elems + halo] = right_ref[...]
    gathered = dot(ext_ref[...], sel_ref[...])
    blocks = members * 3
    for f in range(4):
        jump = (gathered[:, f * elems:(f + 1) * elems] - msk_ref[f:f + 1, :] * own) * fs_ref[f:f + 1, :]
        for b in range(blocks):
            x_ref[(2 + f) * nodes:(3 + f) * nodes, b * elems:(b + 1) * elems] = jump[b * nodes:(b + 1) * nodes]
    for m in range(members):
        comps = [own[(m * 3 + d) * nodes:(m * 3 + d + 1) * nodes] for d in range(3)]
        for dirn in range(2):
            for c in range(3):
                v = (fm_ref[dirn, 0, c] * comps[0] + fm_ref[dirn, 1, c] * comps[1]
                     + fm_ref[dirn, 2, c] * comps[2])
                b = m * 3 + c
                x_ref[dirn * nodes:(dirn + 1) * nodes, b * elems:(b + 1) * elems] = geo_ref[dirn:dirn + 1, :] * v
    out = dot(w_ref[...], x_ref[...])
    wet = wet_ref[...].astype(jnp.float32)
    coef = coef_ref[...]
    wts = wts_ref[...]
    acc = acc_ref[...]

    def work(m, state_rows):
        m0 = mom_ref[(m * 2) * nodes:(m * 2 + 1) * nodes, :].astype(jnp.float32)
        m1 = mom_ref[(m * 2 + 1) * nodes:(m * 2 + 2) * nodes, :].astype(jnp.float32)
        term = wts * (m0 * state_rows[1] + m1 * state_rows[2])
        return jnp.sum(term, axis=0, keepdims=True)

    gains = []
    for m in range(members):
        news = []
        for c in range(3):
            b = m * 3 + c
            rows_b = slice(b * nodes, (b + 1) * nodes)
            r = out[:, b * elems:(b + 1) * elems]
            if c > 0:
                r = r - coef * own[rows_b]
            stepped = own[rows_b] + TIME_STEP * (wet * r)
            if mode == 1:
                stepped = 0.5 * base_ref[rows_b, :] + 0.5 * stepped
            out_ref[rows_b, :] = stepped
            news.append(stepped)
        gain = acc[m:m + 1, :]
        if work_in:
            gain = gain + work(m, [own[(m * 3 + d) * nodes:(m * 3 + d + 1) * nodes] for d in range(3)])
        if work_out:
            gain = gain + work(m, news)
        gains.append(gain)
    acc_out_ref[...] = jnp.concatenate(gains, axis=0)


def rhs_call(mode, work_in, work_out, fm, own, left, right, base, sel, msk, fs, geo, coef, wet, w, mom, wts, acc,
             members, nodes, elems):
    rows = members * 3 * nodes
    vmem = pl.BlockSpec(memory_space=pltpu.VMEM)
    return pl.pallas_call(
        functools.partial(rhs_kernel, members, nodes, elems, mode, work_in, work_out),
        out_shape=(jax.ShapeDtypeStruct((rows, elems), jnp.float32),
                   jax.ShapeDtypeStruct((members, elems), jnp.float32)),
        in_specs=[pl.BlockSpec(memory_space=pltpu.SMEM)] + [vmem] * 14,
        out_specs=(vmem, vmem),
        scratch_shapes=[pltpu.VMEM((rows, 3 * elems), jnp.float32),
                        pltpu.VMEM((6 * nodes, members * 3 * elems), jnp.float32)],
    )(fm, own, left, right, base, sel, msk, fs, geo, coef, wet, w, mom, wts, acc)


def friction_work(adjoint_now, moment, weights):
    return jnp.sum(
        weights * (moment[:, 0] * adjoint_now[:, 1] + moment[:, 1] * adjoint_now[:, 2]), axis=1
    )


def shards(
    adjoint,
    momentum,
    friction,
    roughness,
    geometry,
    face_scale,
    vol_blocks,
    face_blocks,
    flux_mix,
    neighbours,
    patch_map,
    patch_owner,
    wet,
):
    members, comps, nodes, elems = adjoint.shape
    rows = members * comps * nodes
    global_start = lax.axis_index("reach") * elems
    patch_rough = roughness[patch_map]
    coef_own = patch_rough[None, :] ** 2 * friction
    wet_own = wet.astype(jnp.float32)
    weights = wet_own * (-2.0 * patch_rough) * friction

    position = neighbours - global_start
    valid = neighbours >= 0
    row_of = jnp.where(position < 0, position + elems + RIVW,
                       jnp.where(position >= elems, position + elems, position))
    src = jnp.arange(3 * elems, dtype=jnp.int32)
    sel = (src[:, None, None] == row_of[None, :, :]) & valid[None, :, :]
    sel = sel.reshape(3 * elems, 4 * elems).astype(jnp.float32)
    msk = valid.astype(jnp.float32)
    blocks = jnp.concatenate([vol_blocks[0], vol_blocks[1]] + [face_blocks[f] for f in range(4)], axis=1)
    wet_row = wet[None, :]
    mom = momentum.reshape(members * 2 * nodes, elems)

    def stage(mode, work_in, work_out, state, base, acc):
        left, right = halos(state, "reach", RIVW)
        return rhs_call(mode, work_in, work_out, flux_mix, state, left, right, base, sel, msk, face_scale,
                        geometry, coef_own, wet_row, blocks, mom, weights, acc, members, nodes, elems)

    adjoint_now = adjoint.reshape(rows, elems)
    accrued = jnp.zeros((members, elems), jnp.float32)
    for step_no in range(STEPS):
        first = step_no == 0
        last = step_no == STEPS - 1
        halfway, accrued = stage(0, first, True, adjoint_now, adjoint_now, accrued)
        adjoint_now, accrued = stage(1, False, not last, halfway, adjoint_now, accrued)
    adjoint_now = adjoint_now.reshape(members, comps, nodes, elems)
    per_element = jnp.sum(accrued, axis=0)
    owner_count = lax.axis_size("reach")
    total_members = members * lax.axis_size("ens")
    patch_count = roughness.shape[0]
    patch_ids = jnp.arange(patch_count, dtype=jnp.int32)
    owner_e = patch_owner[patch_map]
    earlier = (patch_ids[None, :] < patch_map[:, None]) & (patch_owner[None, :] == owner_e[:, None])
    rank_e = jnp.sum(earlier.astype(jnp.int32), axis=1)
    slot_e = owner_e * OWN_MAX + rank_e
    slot_ids = jnp.arange(owner_count * OWN_MAX, dtype=jnp.int32)
    hit = slot_e[None, :] == slot_ids[:, None]
    send = jnp.sum(jnp.where(hit, per_element[None, :], 0.0), axis=1).reshape(owner_count, OWN_MAX)
    got = lax.all_to_all(send, "reach", 0, 0, tiled=True)
    owned = lax.psum(jnp.sum(got, axis=0), "ens") / (total_members * nodes)
    return (adjoint_now, owned)


def solution(mesh):
    return jax.shard_map(
        shards,
        mesh=mesh,
        in_specs=(
            P("ens", None, None, "reach"),
            P("ens", None, None, "reach"),
            P(None, "reach"),
            P(),
            P(None, "reach"),
            P(None, "reach"),
            P(),
            P(),
            P(),
            P(None, "reach"),
            P("reach"),
            P(),
            P("reach"),
        ),
        out_specs=(P("ens", None, None, "reach"), P("reach")),
        check_vma=False,
    )
```

```python
import functools

import jax
import jax.numpy as jnp
from jax import lax
from jax.experimental import pallas as pl
from jax.experimental.pallas import tpu as pltpu
from jax.sharding import PartitionSpec as P

RIVW = 32
STEPS = 2
OWN_MAX = 32

TIME_STEP = 0.05


def halos(cells, axis, width):
    count = lax.axis_size(axis)
    ends = count - 1
    head = lax.slice_in_dim(cells, 0, width, axis=1)
    tail = lax.slice_in_dim(cells, cells.shape[1] - width, cells.shape[1], axis=1)
    left = lax.ppermute(tail, axis, [(i, (i + 1) % count) for i in range(ends)])
    right = lax.ppermute(head, axis, [((i + 1) % count, i) for i in range(ends)])
    return left, right


def rhs_kernel(members, nodes, elems, mode, work_in, work_out, fm_ref, own_ref, left_ref, right_ref, base_ref,
               sel_ref, msk_ref, fs_ref, geo_ref, coef_ref, wet_ref, w_ref, mom_ref, wts_ref, acc_ref,
               out_ref, acc_out_ref, ext_ref, x_ref):
    dot = functools.partial(jnp.dot, preferred_element_type=jnp.float32, precision=lax.Precision.HIGHEST)
    rows = own_ref.shape[0]
    halo = left_ref.shape[1]
    own = own_ref[...]
    ext_ref[:, 0:elems] = own
    ext_ref[:, elems:3 * elems] = jnp.zeros((rows, 2 * elems), jnp.float32)
    ext_ref[:, elems:elems + halo] = left_ref[...]
    ext_ref[:, 2 * elems:2 * elems + halo] = right_ref[...]
    gathered = dot(ext_ref[...], sel_ref[...])
    blocks = members * 3
    for f in range(4):
        jump = (gathered[:, f * elems:(f + 1) * elems] - msk_ref[f:f + 1, :] * own) * fs_ref[f:f + 1, :]
        for b in range(blocks):
            x_ref[(2 + f) * nodes:(3 + f) * nodes, b * elems:(b + 1) * elems] = jump[b * nodes:(b + 1) * nodes]
    for m in range(members):
        comps = [own[(m * 3 + d) * nodes:(m * 3 + d + 1) * nodes] for d in range(3)]
        for dirn in range(2):
            for c in range(3):
                v = (fm_ref[dirn, 0, c] * comps[0] + fm_ref[dirn, 1, c] * comps[1]
                     + fm_ref[dirn, 2, c] * comps[2])
                b = m * 3 + c
                x_ref[dirn * nodes:(dirn + 1) * nodes, b * elems:(b + 1) * elems] = geo_ref[dirn:dirn + 1, :] * v
    out = dot(w_ref[...], x_ref[...])
    wet = wet_ref[...].astype(jnp.float32)
    coef = coef_ref[...]
    wts = wts_ref[...]
    acc = acc_ref[...]

    def work(m, state_rows):
        m0 = mom_ref[(m * 2) * nodes:(m * 2 + 1) * nodes, :].astype(jnp.float32)
        m1 = mom_ref[(m * 2 + 1) * nodes:(m * 2 + 2) * nodes, :].astype(jnp.float32)
        term = wts * (m0 * state_rows[1] + m1 * state_rows[2])
        return jnp.sum(term, axis=0, keepdims=True)

    gains = []
    for m in range(members):
        news = []
        for c in range(3):
            b = m * 3 + c
            rows_b = slice(b * nodes, (b + 1) * nodes)
            r = out[:, b * elems:(b + 1) * elems]
            if c > 0:
                r = r - coef * own[rows_b]
            stepped = own[rows_b] + TIME_STEP * (wet * r)
            if mode == 1:
                stepped = 0.5 * base_ref[rows_b, :] + 0.5 * stepped
            out_ref[rows_b, :] = stepped
            news.append(stepped)
        gain = acc[m:m + 1, :]
        if work_in:
            gain = gain + work(m, [own[(m * 3 + d) * nodes:(m * 3 + d + 1) * nodes] for d in range(3)])
        if work_out:
            gain = gain + work(m, news)
        gains.append(gain)
    acc_out_ref[...] = jnp.concatenate(gains, axis=0)


def rhs_call(mode, work_in, work_out, fm, own, left, right, base, sel, msk, fs, geo, coef, wet, w, mom, wts, acc,
             members, nodes, elems):
    rows = members * 3 * nodes
    vmem = pl.BlockSpec(memory_space=pltpu.VMEM)
    return pl.pallas_call(
        functools.partial(rhs_kernel, members, nodes, elems, mode, work_in, work_out),
        out_shape=(jax.ShapeDtypeStruct((rows, elems), jnp.float32),
                   jax.ShapeDtypeStruct((members, elems), jnp.float32)),
        in_specs=[pl.BlockSpec(memory_space=pltpu.SMEM)] + [vmem] * 14,
        out_specs=(vmem, vmem),
        scratch_shapes=[pltpu.VMEM((rows, 3 * elems), jnp.float32),
                        pltpu.VMEM((6 * nodes, members * 3 * elems), jnp.float32)],
    )(fm, own, left, right, base, sel, msk, fs, geo, coef, wet, w, mom, wts, acc)


def friction_work(adjoint_now, moment, weights):
    return jnp.sum(
        weights * (moment[:, 0] * adjoint_now[:, 1] + moment[:, 1] * adjoint_now[:, 2]), axis=1
    )


def shards(
    adjoint,
    momentum,
    friction,
    roughness,
    geometry,
    face_scale,
    vol_blocks,
    face_blocks,
    flux_mix,
    neighbours,
    patch_map,
    patch_owner,
    wet,
):
    members, comps, nodes, elems = adjoint.shape
    rows = members * comps * nodes
    global_start = lax.axis_index("reach") * elems
    patch_rough = roughness[patch_map]
    coef_own = patch_rough[None, :] ** 2 * friction
    wet_own = wet.astype(jnp.float32)
    weights = wet_own * (-2.0 * patch_rough) * friction

    position = neighbours - global_start
    valid = neighbours >= 0
    row_of = jnp.where(position < 0, position + elems + RIVW,
                       jnp.where(position >= elems, position + elems, position))
    src = jnp.arange(3 * elems, dtype=jnp.int32)
    sel = (src[:, None, None] == row_of[None, :, :]) & valid[None, :, :]
    sel = sel.reshape(3 * elems, 4 * elems).astype(jnp.float32)
    msk = valid.astype(jnp.float32)
    blocks = jnp.concatenate([vol_blocks[0], vol_blocks[1]] + [face_blocks[f] for f in range(4)], axis=1)
    wet_row = wet[None, :]
    mom = momentum.reshape(members * 2 * nodes, elems)

    def stage(mode, work_in, work_out, state, base, acc):
        left, right = halos(state, "reach", RIVW)
        return rhs_call(mode, work_in, work_out, flux_mix, state, left, right, base, sel, msk, face_scale,
                        geometry, coef_own, wet_row, blocks, mom, weights, acc, members, nodes, elems)

    def route(accrued):
        per_element = jnp.sum(accrued, axis=0)
        owner_count = lax.axis_size("reach")
        total_members = members * lax.axis_size("ens")
        patch_count = roughness.shape[0]
        patch_ids = jnp.arange(patch_count, dtype=jnp.int32)
        owner_e = patch_owner[patch_map]
        earlier = (patch_ids[None, :] < patch_map[:, None]) & (patch_owner[None, :] == owner_e[:, None])
        rank_e = jnp.sum(earlier.astype(jnp.int32), axis=1)
        slot_e = owner_e * OWN_MAX + rank_e
        slot_ids = jnp.arange(owner_count * OWN_MAX, dtype=jnp.int32)
        hit = slot_e[None, :] == slot_ids[:, None]
        send = jnp.sum(jnp.where(hit, per_element[None, :], 0.0), axis=1).reshape(owner_count, OWN_MAX)
        got = lax.all_to_all(send, "reach", 0, 0, tiled=True)
        owned = lax.psum(jnp.sum(got, axis=0), "ens") / (total_members * nodes)
        return owned

    adjoint_now = adjoint.reshape(rows, elems)
    accrued = jnp.zeros((members, elems), jnp.float32)
    owned = None
    for step_no in range(STEPS):
        first = step_no == 0
        last = step_no == STEPS - 1
        halfway, accrued = stage(0, first, True, adjoint_now, adjoint_now, accrued)
        if last:
            owned = route(accrued)
            owned, halfway, adjoint_now = lax.optimization_barrier((owned, halfway, adjoint_now))
        adjoint_now, accrued = stage(1, False, not last, halfway, adjoint_now, accrued)
    adjoint_now = adjoint_now.reshape(members, comps, nodes, elems)
    return (adjoint_now, owned)


def solution(mesh):
    return jax.shard_map(
        shards,
        mesh=mesh,
        in_specs=(
            P("ens", None, None, "reach"),
            P("ens", None, None, "reach"),
            P(None, "reach"),
            P(),
            P(None, "reach"),
            P(None, "reach"),
            P(),
            P(),
            P(),
            P(None, "reach"),
            P("reach"),
            P(),
            P("reach"),
        ),
        out_specs=(P("ens", None, None, "reach"), P("reach")),
        check_vma=False,
    )
```

```python
import functools

import jax
import jax.numpy as jnp
from jax import lax
from jax.experimental import pallas as pl
from jax.experimental.pallas import tpu as pltpu
from jax.sharding import PartitionSpec as P

RIVW = 32
STEPS = 2
OWN_MAX = 32
PAD = 128

TIME_STEP = 0.05


def halos(cells, axis, width):
    count = lax.axis_size(axis)
    ends = count - 1
    head = lax.slice_in_dim(cells, 0, width, axis=1)
    tail = lax.slice_in_dim(cells, cells.shape[1] - width, cells.shape[1], axis=1)
    left = lax.ppermute(tail, axis, [(i, (i + 1) % count) for i in range(ends)])
    right = lax.ppermute(head, axis, [((i + 1) % count, i) for i in range(ends)])
    return left, right


def rhs_kernel(members, nodes, elems, fm_ref, ext_ref, sel_ref, msk_ref, fs_ref, geo_ref, coef_ref,
               wet_ref, w_ref, out_ref, x_ref):
    dot = functools.partial(jnp.dot, preferred_element_type=jnp.float32, precision=lax.Precision.HIGH)
    ext = ext_ref[...]
    own = ext[:, PAD:PAD + elems]
    sel = sel_ref[...]
    gathered = dot(ext, sel)
    blocks = members * 3
    for f in range(4):
        jump = (gathered[:, f * elems:(f + 1) * elems] - msk_ref[f:f + 1, :] * own) * fs_ref[f:f + 1, :]
        for b in range(blocks):
            x_ref[(2 + f) * nodes:(3 + f) * nodes, b * elems:(b + 1) * elems] = jump[b * nodes:(b + 1) * nodes]
    for m in range(members):
        comps = [own[(m * 3 + d) * nodes:(m * 3 + d + 1) * nodes] for d in range(3)]
        for dirn in range(2):
            for c in range(3):
                v = (fm_ref[dirn * 9 + c] * comps[0] + fm_ref[dirn * 9 + 3 + c] * comps[1]
                     + fm_ref[dirn * 9 + 6 + c] * comps[2])
                b = m * 3 + c
                x_ref[dirn * nodes:(dirn + 1) * nodes, b * elems:(b + 1) * elems] = geo_ref[dirn:dirn + 1, :] * v
    out = dot(w_ref[...], x_ref[...])
    wet = wet_ref[...]
    coef = coef_ref[...]
    for b in range(blocks):
        r = out[:, b * elems:(b + 1) * elems]
        if b % 3 > 0:
            r = r - coef * own[b * nodes:(b + 1) * nodes]
        out_ref[b * nodes:(b + 1) * nodes, :] = wet * r


def rhs_call(fm, ext, sel, msk, fs, geo, coef, wet, w, members, nodes, elems):
    rows = members * 3 * nodes
    vmem = pl.BlockSpec(memory_space=pltpu.VMEM)
    return pl.pallas_call(
        functools.partial(rhs_kernel, members, nodes, elems),
        out_shape=jax.ShapeDtypeStruct((rows, elems), jnp.float32),
        in_specs=[pl.BlockSpec(memory_space=pltpu.SMEM)] + [vmem] * 8,
        out_specs=vmem,
        scratch_shapes=[pltpu.VMEM((6 * nodes, members * 3 * elems), jnp.float32)],
    )(fm, ext, sel, msk, fs, geo, coef, wet, w)


def friction_work(adjoint_now, moment, weights):
    return jnp.sum(
        weights * (moment[:, 0] * adjoint_now[:, 1] + moment[:, 1] * adjoint_now[:, 2]), axis=1
    )


def shards(
    adjoint,
    momentum,
    friction,
    roughness,
    geometry,
    face_scale,
    vol_blocks,
    face_blocks,
    flux_mix,
    neighbours,
    patch_map,
    patch_owner,
    wet,
):
    members, comps, nodes, elems = adjoint.shape
    rows = members * comps * nodes
    global_start = lax.axis_index("reach") * elems
    patch_rough = roughness[patch_map]
    coef_own = patch_rough[None, :] ** 2 * friction
    wet_own = wet.astype(jnp.float32)
    weights = wet_own * (-2.0 * patch_rough) * friction
    moment = momentum.astype(jnp.float32)

    width = elems + 2 * PAD
    position = neighbours - global_start + PAD
    valid = neighbours >= 0
    src = jnp.arange(width, dtype=jnp.int32)
    sel = (src[:, None, None] == position[None, :, :]) & valid[None, :, :]
    sel = sel.reshape(width, 4 * elems).astype(jnp.float32)
    msk = valid.astype(jnp.float32)
    blocks = jnp.concatenate([vol_blocks[0], vol_blocks[1]] + [face_blocks[f] for f in range(4)], axis=1)
    fm = flux_mix.reshape(-1)
    wet_row = wet_own[None, :]

    def section_slope(state):
        flat = state.reshape(rows, elems)
        left, right = halos(flat, "reach", RIVW)
        zeros = jnp.zeros((rows, PAD - RIVW), jnp.float32)
        ext = jnp.concatenate([zeros, left, flat, right, zeros], axis=1)
        slope = rhs_call(fm, ext, sel, msk, face_scale, geometry, coef_own, wet_row, blocks,
                         members, nodes, elems)
        return slope.reshape(members, comps, nodes, elems)

    adjoint_now = adjoint
    accrued = jnp.zeros((members, elems), jnp.float32)
    for step_no in range(STEPS):
        accrued = accrued + friction_work(adjoint_now, moment, weights)
        halfway = adjoint_now + TIME_STEP * section_slope(adjoint_now)
        accrued = accrued + friction_work(halfway, moment, weights)
        adjoint_now = 0.5 * adjoint_now + 0.5 * (halfway + TIME_STEP * section_slope(halfway))
    per_element = jnp.sum(accrued, axis=0)
    owner_count = lax.axis_size("reach")
    total_members = members * lax.axis_size("ens")
    patch_count = roughness.shape[0]
    patch_ids = jnp.arange(patch_count, dtype=jnp.int32)
    owner_e = patch_owner[patch_map]
    earlier = (patch_ids[None, :] < patch_map[:, None]) & (patch_owner[None, :] == owner_e[:, None])
    rank_e = jnp.sum(earlier.astype(jnp.int32), axis=1)
    slot_e = owner_e * OWN_MAX + rank_e
    slot_ids = jnp.arange(owner_count * OWN_MAX, dtype=jnp.int32)
    hit = slot_e[None, :] == slot_ids[:, None]
    send = jnp.sum(jnp.where(hit, per_element[None, :], 0.0), axis=1).reshape(owner_count, OWN_MAX)
    got = lax.all_to_all(send, "reach", 0, 0, tiled=True)
    owned = lax.psum(jnp.sum(got, axis=0), "ens") / (total_members * nodes)
    return (adjoint_now, owned)


def solution(mesh):
    return jax.shard_map(
        shards,
        mesh=mesh,
        in_specs=(
            P("ens", None, None, "reach"),
            P("ens", None, None, "reach"),
            P(None, "reach"),
            P(),
            P(None, "reach"),
            P(None, "reach"),
            P(),
            P(),
            P(),
            P(None, "reach"),
            P("reach"),
            P(),
            P("reach"),
        ),
        out_specs=(P("ens", None, None, "reach"), P("reach")),
        check_vma=False,
    )
```

```python
import functools

import jax
import jax.numpy as jnp
from jax import lax
from jax.experimental import pallas as pl
from jax.experimental.pallas import tpu as pltpu
from jax.sharding import PartitionSpec as P

RIVW = 32
STEPS = 2
OWN_MAX = 32

TIME_STEP = 0.05


def halos(cells, axis, width):
    count = lax.axis_size(axis)
    ends = count - 1
    head = lax.slice_in_dim(cells, 0, width, axis=1)
    tail = lax.slice_in_dim(cells, cells.shape[1] - width, cells.shape[1], axis=1)
    left = lax.ppermute(tail, axis, [(i, (i + 1) % count) for i in range(ends)])
    right = lax.ppermute(head, axis, [((i + 1) % count, i) for i in range(ends)])
    return left, right


def rhs_kernel(members, nodes, elems, mode, work_in, work_out, fm_ref, own_ref, left_ref, right_ref, base_ref,
               sel_ref, msk_ref, fs_ref, geo_ref, coef_ref, wet_ref, w_ref, mom_ref, wts_ref, acc_ref,
               out_ref, acc_out_ref, ext_ref, x_ref):
    dot = functools.partial(jnp.dot, preferred_element_type=jnp.float32, precision=lax.Precision.HIGH)
    rows = own_ref.shape[0]
    halo = left_ref.shape[1]
    own = own_ref[...]
    ext_ref[:, 0:elems] = own
    ext_ref[:, elems:3 * elems] = jnp.zeros((rows, 2 * elems), jnp.float32)
    ext_ref[:, elems:elems + halo] = left_ref[...]
    ext_ref[:, 2 * elems:2 * elems + halo] = right_ref[...]
    gathered = dot(ext_ref[...], sel_ref[...])
    blocks = members * 3
    for f in range(4):
        jump = (gathered[:, f * elems:(f + 1) * elems] - msk_ref[f:f + 1, :] * own) * fs_ref[f:f + 1, :]
        for b in range(blocks):
            x_ref[(2 + f) * nodes:(3 + f) * nodes, b * elems:(b + 1) * elems] = jump[b * nodes:(b + 1) * nodes]
    for m in range(members):
        comps = [own[(m * 3 + d) * nodes:(m * 3 + d + 1) * nodes] for d in range(3)]
        for dirn in range(2):
            for c in range(3):
                v = (fm_ref[dirn, 0, c] * comps[0] + fm_ref[dirn, 1, c] * comps[1]
                     + fm_ref[dirn, 2, c] * comps[2])
                b = m * 3 + c
                x_ref[dirn * nodes:(dirn + 1) * nodes, b * elems:(b + 1) * elems] = geo_ref[dirn:dirn + 1, :] * v
    out = dot(w_ref[...], x_ref[...])
    wet = wet_ref[...].astype(jnp.float32)
    coef = coef_ref[...]
    wts = wts_ref[...]
    acc = acc_ref[...]

    def work(m, state_rows):
        m0 = mom_ref[(m * 2) * nodes:(m * 2 + 1) * nodes, :].astype(jnp.float32)
        m1 = mom_ref[(m * 2 + 1) * nodes:(m * 2 + 2) * nodes, :].astype(jnp.float32)
        term = wts * (m0 * state_rows[1] + m1 * state_rows[2])
        return jnp.sum(term, axis=0, keepdims=True)

    gains = []
    for m in range(members):
        news = []
        for c in range(3):
            b = m * 3 + c
            rows_b = slice(b * nodes, (b + 1) * nodes)
            r = out[:, b * elems:(b + 1) * elems]
            if c > 0:
                r = r - coef * own[rows_b]
            stepped = own[rows_b] + TIME_STEP * (wet * r)
            if mode == 1:
                stepped = 0.5 * base_ref[rows_b, :] + 0.5 * stepped
            out_ref[rows_b, :] = stepped
            news.append(stepped)
        gain = acc[m:m + 1, :]
        if work_in:
            gain = gain + work(m, [own[(m * 3 + d) * nodes:(m * 3 + d + 1) * nodes] for d in range(3)])
        if work_out:
            gain = gain + work(m, news)
        gains.append(gain)
    acc_out_ref[...] = jnp.concatenate(gains, axis=0)


def rhs_call(mode, work_in, work_out, fm, own, left, right, base, sel, msk, fs, geo, coef, wet, w, mom, wts, acc,
             members, nodes, elems):
    rows = members * 3 * nodes
    vmem = pl.BlockSpec(memory_space=pltpu.VMEM)
    return pl.pallas_call(
        functools.partial(rhs_kernel, members, nodes, elems, mode, work_in, work_out),
        out_shape=(jax.ShapeDtypeStruct((rows, elems), jnp.float32),
                   jax.ShapeDtypeStruct((members, elems), jnp.float32)),
        in_specs=[pl.BlockSpec(memory_space=pltpu.SMEM)] + [vmem] * 14,
        out_specs=(vmem, vmem),
        scratch_shapes=[pltpu.VMEM((rows, 3 * elems), jnp.float32),
                        pltpu.VMEM((6 * nodes, members * 3 * elems), jnp.float32)],
    )(fm, own, left, right, base, sel, msk, fs, geo, coef, wet, w, mom, wts, acc)


def friction_work(adjoint_now, moment, weights):
    return jnp.sum(
        weights * (moment[:, 0] * adjoint_now[:, 1] + moment[:, 1] * adjoint_now[:, 2]), axis=1
    )


def shards(
    adjoint,
    momentum,
    friction,
    roughness,
    geometry,
    face_scale,
    vol_blocks,
    face_blocks,
    flux_mix,
    neighbours,
    patch_map,
    patch_owner,
    wet,
):
    members, comps, nodes, elems = adjoint.shape
    rows = members * comps * nodes
    global_start = lax.axis_index("reach") * elems
    patch_rough = roughness[patch_map]
    coef_own = patch_rough[None, :] ** 2 * friction
    wet_own = wet.astype(jnp.float32)
    weights = wet_own * (-2.0 * patch_rough) * friction

    position = neighbours - global_start
    valid = neighbours >= 0
    row_of = jnp.where(position < 0, position + elems + RIVW,
                       jnp.where(position >= elems, position + elems, position))
    src = jnp.arange(3 * elems, dtype=jnp.int32)
    sel = (src[:, None, None] == row_of[None, :, :]) & valid[None, :, :]
    sel = sel.reshape(3 * elems, 4 * elems).astype(jnp.float32)
    msk = valid.astype(jnp.float32)
    blocks = jnp.concatenate([vol_blocks[0], vol_blocks[1]] + [face_blocks[f] for f in range(4)], axis=1)
    wet_row = wet[None, :]
    mom = momentum.reshape(members * 2 * nodes, elems)

    def stage(mode, work_in, work_out, state, base, acc, halo=None):
        left, right = halos(state, "reach", RIVW) if halo is None else halo
        return rhs_call(mode, work_in, work_out, flux_mix, state, left, right, base, sel, msk, face_scale,
                        geometry, coef_own, wet_row, blocks, mom, weights, acc, members, nodes, elems)

    def route(accrued):
        per_element = jnp.sum(accrued, axis=0)
        owner_count = lax.axis_size("reach")
        total_members = members * lax.axis_size("ens")
        patch_count = roughness.shape[0]
        patch_ids = jnp.arange(patch_count, dtype=jnp.int32)
        owner_e = patch_owner[patch_map]
        earlier = (patch_ids[None, :] < patch_map[:, None]) & (patch_owner[None, :] == owner_e[:, None])
        rank_e = jnp.sum(earlier.astype(jnp.int32), axis=1)
        slot_e = owner_e * OWN_MAX + rank_e
        slot_ids = jnp.arange(owner_count * OWN_MAX, dtype=jnp.int32)
        hit = slot_e[None, :] == slot_ids[:, None]
        send = jnp.sum(jnp.where(hit, per_element[None, :], 0.0), axis=1).reshape(owner_count, OWN_MAX)
        got = lax.all_to_all(send, "reach", 0, 0, tiled=True)
        owned = lax.psum(jnp.sum(got, axis=0), "ens") / (total_members * nodes)
        return owned

    adjoint_now = adjoint.reshape(rows, elems)
    accrued = jnp.zeros((members, elems), jnp.float32)
    owned = None
    for step_no in range(STEPS):
        first = step_no == 0
        last = step_no == STEPS - 1
        halfway, accrued = stage(0, first, True, adjoint_now, adjoint_now, accrued)
        halo = None
        if last:
            halo = halos(halfway, "reach", RIVW)
            owned = route(accrued)
            owned, halfway, adjoint_now = lax.optimization_barrier((owned, halfway, adjoint_now))
        adjoint_now, accrued = stage(1, False, not last, halfway, adjoint_now, accrued, halo)
    adjoint_now = adjoint_now.reshape(members, comps, nodes, elems)
    return (adjoint_now, owned)


def solution(mesh):
    return jax.shard_map(
        shards,
        mesh=mesh,
        in_specs=(
            P("ens", None, None, "reach"),
            P("ens", None, None, "reach"),
            P(None, "reach"),
            P(),
            P(None, "reach"),
            P(None, "reach"),
            P(),
            P(),
            P(),
            P(None, "reach"),
            P("reach"),
            P(),
            P("reach"),
        ),
        out_specs=(P("ens", None, None, "reach"), P("reach")),
        check_vma=False,
    )
```

```python
import functools

import jax
import jax.numpy as jnp
from jax import lax
from jax.experimental import pallas as pl
from jax.experimental.pallas import tpu as pltpu
from jax.sharding import PartitionSpec as P

RIVW = 32
STEPS = 2
OWN_MAX = 32

TIME_STEP = 0.05


def halos(head, tail, axis):
    count = lax.axis_size(axis)
    ends = count - 1
    left = lax.ppermute(tail, axis, [(i, (i + 1) % count) for i in range(ends)])
    right = lax.ppermute(head, axis, [((i + 1) % count, i) for i in range(ends)])
    return left, right


def rhs_kernel(members, nodes, elems, mode, work_in, work_out, fm_ref, own_ref, left_ref, right_ref, base_ref,
               sel_ref, msk_ref, fs_ref, geo_ref, coef_ref, wet_ref, w_ref, mom_ref, wts_ref, acc_ref,
               out_ref, acc_out_ref, head_ref, tail_ref, ext_ref, x_ref):
    dot = functools.partial(jnp.dot, preferred_element_type=jnp.float32, precision=lax.Precision.HIGH)
    rows = own_ref.shape[0]
    halo = left_ref.shape[1]
    own = own_ref[...]
    ext_ref[:, 0:elems] = own
    ext_ref[:, elems:3 * elems] = jnp.zeros((rows, 2 * elems), jnp.float32)
    ext_ref[:, elems:elems + halo] = left_ref[...]
    ext_ref[:, 2 * elems:2 * elems + halo] = right_ref[...]
    gathered = dot(ext_ref[...], sel_ref[...])
    blocks = members * 3
    for f in range(4):
        jump = (gathered[:, f * elems:(f + 1) * elems] - msk_ref[f:f + 1, :] * own) * fs_ref[f:f + 1, :]
        for b in range(blocks):
            x_ref[(2 + f) * nodes:(3 + f) * nodes, b * elems:(b + 1) * elems] = jump[b * nodes:(b + 1) * nodes]
    for m in range(members):
        comps = [own[(m * 3 + d) * nodes:(m * 3 + d + 1) * nodes] for d in range(3)]
        for dirn in range(2):
            for c in range(3):
                v = (fm_ref[dirn, 0, c] * comps[0] + fm_ref[dirn, 1, c] * comps[1]
                     + fm_ref[dirn, 2, c] * comps[2])
                b = m * 3 + c
                x_ref[dirn * nodes:(dirn + 1) * nodes, b * elems:(b + 1) * elems] = geo_ref[dirn:dirn + 1, :] * v
    out = dot(w_ref[...], x_ref[...])
    wet = wet_ref[...].astype(jnp.float32)
    coef = coef_ref[...]
    wts = wts_ref[...]
    acc = acc_ref[...] if acc_ref is not None else None

    def work(m, state_rows):
        m0 = mom_ref[(m * 2) * nodes:(m * 2 + 1) * nodes, :].astype(jnp.float32)
        m1 = mom_ref[(m * 2 + 1) * nodes:(m * 2 + 2) * nodes, :].astype(jnp.float32)
        term = wts * (m0 * state_rows[1] + m1 * state_rows[2])
        return jnp.sum(term, axis=0, keepdims=True)

    gains = []
    for m in range(members):
        news = []
        for c in range(3):
            b = m * 3 + c
            rows_b = slice(b * nodes, (b + 1) * nodes)
            r = out[:, b * elems:(b + 1) * elems]
            if c > 0:
                r = r - coef * own[rows_b]
            stepped = own[rows_b] + TIME_STEP * (wet * r)
            if mode == 1:
                stepped = 0.5 * base_ref[rows_b, :] + 0.5 * stepped
            out_ref[rows_b, :] = stepped
            news.append(stepped)
        gain = acc[m:m + 1, :] if acc_ref is not None else None
        if work_in:
            add = work(m, [own[(m * 3 + d) * nodes:(m * 3 + d + 1) * nodes] for d in range(3)])
            gain = add if gain is None else gain + add
        if work_out:
            add = work(m, news)
            gain = add if gain is None else gain + add
        gains.append(gain)
    acc_out_ref[...] = jnp.concatenate(gains, axis=0)
    head_ref[...] = out_ref[:, 0:halo]
    tail_ref[...] = out_ref[:, elems - halo:elems]


def rhs_call(mode, work_in, work_out, fm, own, left, right, base, sel, msk, fs, geo, coef, wet, w, mom, wts, acc,
             members, nodes, elems):
    rows = members * 3 * nodes
    halo = left.shape[1]
    vmem = pl.BlockSpec(memory_space=pltpu.VMEM)
    body = functools.partial(rhs_kernel, members, nodes, elems, mode, work_in, work_out)
    inputs = [fm, own, left, right, base, sel, msk, fs, geo, coef, wet, w, mom, wts]
    if acc is None:
        def kernel(*refs):
            return body(*refs[:14], None, *refs[14:])
    else:
        kernel = body
        inputs.append(acc)
    return pl.pallas_call(
        kernel,
        out_shape=(jax.ShapeDtypeStruct((rows, elems), jnp.float32),
                   jax.ShapeDtypeStruct((members, elems), jnp.float32),
                   jax.ShapeDtypeStruct((rows, halo), jnp.float32),
                   jax.ShapeDtypeStruct((rows, halo), jnp.float32)),
        in_specs=[pl.BlockSpec(memory_space=pltpu.SMEM)] + [vmem] * (len(inputs) - 1),
        out_specs=(vmem, vmem, vmem, vmem),
        scratch_shapes=[pltpu.VMEM((rows, 3 * elems), jnp.float32),
                        pltpu.VMEM((6 * nodes, members * 3 * elems), jnp.float32)],
    )(*inputs)


def friction_work(adjoint_now, moment, weights):
    return jnp.sum(
        weights * (moment[:, 0] * adjoint_now[:, 1] + moment[:, 1] * adjoint_now[:, 2]), axis=1
    )


def shards(
    adjoint,
    momentum,
    friction,
    roughness,
    geometry,
    face_scale,
    vol_blocks,
    face_blocks,
    flux_mix,
    neighbours,
    patch_map,
    patch_owner,
    wet,
):
    members, comps, nodes, elems = adjoint.shape
    rows = members * comps * nodes
    global_start = lax.axis_index("reach") * elems
    patch_rough = roughness[patch_map]
    coef_own = patch_rough[None, :] ** 2 * friction
    wet_own = wet.astype(jnp.float32)
    weights = wet_own * (-2.0 * patch_rough) * friction

    position = neighbours - global_start
    valid = neighbours >= 0
    row_of = jnp.where(position < 0, position + elems + RIVW,
                       jnp.where(position >= elems, position + elems, position))
    src = jnp.arange(3 * elems, dtype=jnp.int32)
    sel = (src[:, None, None] == row_of[None, :, :]) & valid[None, :, :]
    sel = sel.reshape(3 * elems, 4 * elems).astype(jnp.float32)
    msk = valid.astype(jnp.float32)
    blocks = jnp.concatenate([vol_blocks[0], vol_blocks[1]] + [face_blocks[f] for f in range(4)], axis=1)
    wet_row = wet[None, :]
    mom = momentum.reshape(members * 2 * nodes, elems)

    def stage(mode, work_in, work_out, state, base, acc, halo):
        left, right = halo
        return rhs_call(mode, work_in, work_out, flux_mix, state, left, right, base, sel, msk, face_scale,
                        geometry, coef_own, wet_row, blocks, mom, weights, acc, members, nodes, elems)

    def route(accrued):
        per_element = jnp.sum(accrued, axis=0)
        owner_count = lax.axis_size("reach")
        total_members = members * lax.axis_size("ens")
        patch_count = roughness.shape[0]
        patch_ids = jnp.arange(patch_count, dtype=jnp.int32)
        owner_e = patch_owner[patch_map]
        earlier = (patch_ids[None, :] < patch_map[:, None]) & (patch_owner[None, :] == owner_e[:, None])
        rank_e = jnp.sum(earlier.astype(jnp.int32), axis=1)
        slot_e = owner_e * OWN_MAX + rank_e
        slot_ids = jnp.arange(owner_count * OWN_MAX, dtype=jnp.int32)
        hit = slot_e[None, :] == slot_ids[:, None]
        send = jnp.sum(jnp.where(hit, per_element[None, :], 0.0), axis=1).reshape(owner_count, OWN_MAX)
        got = lax.all_to_all(send, "reach", 0, 0, tiled=True)
        owned = lax.psum(jnp.sum(got, axis=0), "ens") / (total_members * nodes)
        return owned

    adjoint_now = adjoint.reshape(rows, elems)
    halo = halos(adjoint_now[:, :RIVW], adjoint_now[:, elems - RIVW:], "reach")
    accrued = None
    owned = None
    for step_no in range(STEPS):
        first = step_no == 0
        last = step_no == STEPS - 1
        halfway, accrued, head, tail = stage(0, first, True, adjoint_now, adjoint_now, accrued, halo)
        halo = halos(head, tail, "reach")
        if last:
            owned = route(accrued)
            owned, halfway, adjoint_now = lax.optimization_barrier((owned, halfway, adjoint_now))
        adjoint_now, accrued, head, tail = stage(1, False, not last, halfway, adjoint_now, accrued, halo)
        halo = halos(head, tail, "reach")
    adjoint_now = adjoint_now.reshape(members, comps, nodes, elems)
    return (adjoint_now, owned)


def solution(mesh):
    return jax.shard_map(
        shards,
        mesh=mesh,
        in_specs=(
            P("ens", None, None, "reach"),
            P("ens", None, None, "reach"),
            P(None, "reach"),
            P(),
            P(None, "reach"),
            P(None, "reach"),
            P(),
            P(),
            P(),
            P(None, "reach"),
            P("reach"),
            P(),
            P("reach"),
        ),
        out_specs=(P("ens", None, None, "reach"), P("reach")),
        check_vma=False,
    )
```

```python
import functools

import jax
import jax.numpy as jnp
from jax import lax
from jax.experimental import pallas as pl
from jax.experimental.pallas import tpu as pltpu
from jax.sharding import PartitionSpec as P

RIVW = 32
STEPS = 2
OWN_MAX = 32

TIME_STEP = 0.05


def halos(cells, axis, width):
    count = lax.axis_size(axis)
    ends = count - 1
    head = lax.slice_in_dim(cells, 0, width, axis=1)
    tail = lax.slice_in_dim(cells, cells.shape[1] - width, cells.shape[1], axis=1)
    left = lax.ppermute(tail, axis, [(i, (i + 1) % count) for i in range(ends)])
    right = lax.ppermute(head, axis, [((i + 1) % count, i) for i in range(ends)])
    return left, right


def rhs_kernel(members, nodes, elems, mode, work_in, work_out, fm_ref, own_ref, left_ref, right_ref, base_ref,
               sel_ref, msk_ref, fs_ref, geo_ref, coef_ref, wet_ref, w_ref, mom_ref, wts_ref, acc_ref,
               out_ref, acc_out_ref, ext_ref, x_ref):
    dot = functools.partial(jnp.dot, preferred_element_type=jnp.float32, precision=lax.Precision.HIGH)
    rows = own_ref.shape[0]
    halo = left_ref.shape[1]
    own = own_ref[...]
    ext_ref[:, 0:elems] = own
    ext_ref[:, elems:3 * elems] = jnp.zeros((rows, 2 * elems), jnp.float32)
    ext_ref[:, elems:elems + halo] = left_ref[...]
    ext_ref[:, 2 * elems:2 * elems + halo] = right_ref[...]
    gathered = dot(ext_ref[...], sel_ref[...])
    blocks = members * 3
    for f in range(4):
        jump = (gathered[:, f * elems:(f + 1) * elems] - msk_ref[f:f + 1, :] * own) * fs_ref[f:f + 1, :]
        for b in range(blocks):
            x_ref[(2 + f) * nodes:(3 + f) * nodes, b * elems:(b + 1) * elems] = jump[b * nodes:(b + 1) * nodes]
    for m in range(members):
        comps = [own[(m * 3 + d) * nodes:(m * 3 + d + 1) * nodes] for d in range(3)]
        for dirn in range(2):
            for c in range(3):
                v = (fm_ref[dirn, 0, c] * comps[0] + fm_ref[dirn, 1, c] * comps[1]
                     + fm_ref[dirn, 2, c] * comps[2])
                b = m * 3 + c
                x_ref[dirn * nodes:(dirn + 1) * nodes, b * elems:(b + 1) * elems] = geo_ref[dirn:dirn + 1, :] * v
    out = dot(w_ref[...], x_ref[...])
    wet = wet_ref[...].astype(jnp.float32)
    coef = coef_ref[...]
    wts = wts_ref[...]
    acc = acc_ref[...]

    def work(m, state_rows):
        m0 = mom_ref[(m * 2) * nodes:(m * 2 + 1) * nodes, :].astype(jnp.float32)
        m1 = mom_ref[(m * 2 + 1) * nodes:(m * 2 + 2) * nodes, :].astype(jnp.float32)
        term = wts * (m0 * state_rows[1] + m1 * state_rows[2])
        return jnp.sum(term, axis=0, keepdims=True)

    gains = []
    for m in range(members):
        news = []
        for c in range(3):
            b = m * 3 + c
            rows_b = slice(b * nodes, (b + 1) * nodes)
            r = out[:, b * elems:(b + 1) * elems]
            if c > 0:
                r = r - coef * own[rows_b]
            stepped = own[rows_b] + TIME_STEP * (wet * r)
            if mode == 1:
                stepped = 0.5 * base_ref[rows_b, :] + 0.5 * stepped
            out_ref[rows_b, :] = stepped
            news.append(stepped)
        gain = acc[m:m + 1, :]
        if work_in:
            gain = gain + work(m, [own[(m * 3 + d) * nodes:(m * 3 + d + 1) * nodes] for d in range(3)])
        if work_out:
            gain = gain + work(m, news)
        gains.append(gain)
    acc_out_ref[...] = jnp.concatenate(gains, axis=0)


def rhs_call(mode, work_in, work_out, fm, own, left, right, base, sel, msk, fs, geo, coef, wet, w, mom, wts, acc,
             members, nodes, elems):
    rows = members * 3 * nodes
    vmem = pl.BlockSpec(memory_space=pltpu.VMEM)
    return pl.pallas_call(
        functools.partial(rhs_kernel, members, nodes, elems, mode, work_in, work_out),
        out_shape=(jax.ShapeDtypeStruct((rows, elems), jnp.float32),
                   jax.ShapeDtypeStruct((members, elems), jnp.float32)),
        in_specs=[pl.BlockSpec(memory_space=pltpu.SMEM)] + [vmem] * 14,
        out_specs=(vmem, vmem),
        scratch_shapes=[pltpu.VMEM((rows, 3 * elems), jnp.float32),
                        pltpu.VMEM((6 * nodes, members * 3 * elems), jnp.float32)],
    )(fm, own, left, right, base, sel, msk, fs, geo, coef, wet, w, mom, wts, acc)


def friction_work(adjoint_now, moment, weights):
    return jnp.sum(
        weights * (moment[:, 0] * adjoint_now[:, 1] + moment[:, 1] * adjoint_now[:, 2]), axis=1
    )


def shards(
    adjoint,
    momentum,
    friction,
    roughness,
    geometry,
    face_scale,
    vol_blocks,
    face_blocks,
    flux_mix,
    neighbours,
    patch_map,
    patch_owner,
    wet,
):
    members, comps, nodes, elems = adjoint.shape
    rows = members * comps * nodes
    global_start = lax.axis_index("reach") * elems
    patch_rough = roughness[patch_map]
    coef_own = patch_rough[None, :] ** 2 * friction
    wet_own = wet.astype(jnp.float32)
    weights = wet_own * (-2.0 * patch_rough) * friction

    position = neighbours - global_start
    valid = neighbours >= 0
    row_of = jnp.where(position < 0, position + elems + RIVW,
                       jnp.where(position >= elems, position + elems, position))
    src = jnp.arange(3 * elems, dtype=jnp.int32)
    sel = (src[:, None, None] == row_of[None, :, :]) & valid[None, :, :]
    sel = sel.reshape(3 * elems, 4 * elems).astype(jnp.float32)
    msk = valid.astype(jnp.float32)
    blocks = jnp.concatenate([vol_blocks[0], vol_blocks[1]] + [face_blocks[f] for f in range(4)], axis=1)
    wet_row = wet[None, :]
    mom = momentum.reshape(members * 2 * nodes, elems)

    def stage(mode, work_in, work_out, state, base, acc, halo=None):
        left, right = halos(state, "reach", RIVW) if halo is None else halo
        return rhs_call(mode, work_in, work_out, flux_mix, state, left, right, base, sel, msk, face_scale,
                        geometry, coef_own, wet_row, blocks, mom, weights, acc, members, nodes, elems)

    def route(accrued, patch_map):
        per_element = jnp.sum(accrued, axis=0)
        owner_count = lax.axis_size("reach")
        total_members = members * lax.axis_size("ens")
        patch_count = roughness.shape[0]
        patch_ids = jnp.arange(patch_count, dtype=jnp.int32)
        owner_e = patch_owner[patch_map]
        earlier = (patch_ids[None, :] < patch_map[:, None]) & (patch_owner[None, :] == owner_e[:, None])
        rank_e = jnp.sum(earlier.astype(jnp.int32), axis=1)
        slot_e = owner_e * OWN_MAX + rank_e
        slot_ids = jnp.arange(owner_count * OWN_MAX, dtype=jnp.int32)
        hit = slot_e[None, :] == slot_ids[:, None]
        send = jnp.sum(jnp.where(hit, per_element[None, :], 0.0), axis=1).reshape(owner_count, OWN_MAX)
        got = lax.all_to_all(send, "reach", 0, 0, tiled=True)
        owned = lax.psum(jnp.sum(got, axis=0), "ens") / (total_members * nodes)
        return owned

    adjoint_now = adjoint.reshape(rows, elems)
    accrued = jnp.zeros((members, elems), jnp.float32)
    owned = None
    for step_no in range(STEPS):
        first = step_no == 0
        last = step_no == STEPS - 1
        halfway, accrued = stage(0, first, True, adjoint_now, adjoint_now, accrued)
        if first:
            patch_late, accrued = lax.optimization_barrier((patch_map, accrued))
        halo = None
        if last:
            halo = halos(halfway, "reach", RIVW)
            owned = route(accrued, patch_late)
            owned, halfway, adjoint_now = lax.optimization_barrier((owned, halfway, adjoint_now))
        adjoint_now, accrued = stage(1, False, not last, halfway, adjoint_now, accrued, halo)
    adjoint_now = adjoint_now.reshape(members, comps, nodes, elems)
    return (adjoint_now, owned)


def solution(mesh):
    return jax.shard_map(
        shards,
        mesh=mesh,
        in_specs=(
            P("ens", None, None, "reach"),
            P("ens", None, None, "reach"),
            P(None, "reach"),
            P(),
            P(None, "reach"),
            P(None, "reach"),
            P(),
            P(),
            P(),
            P(None, "reach"),
            P("reach"),
            P(),
            P("reach"),
        ),
        out_specs=(P("ens", None, None, "reach"), P("reach")),
        check_vma=False,
    )
```
